768 devices in a mesh: dp: 128 (over y, x, z_hi, core), space: 6 (over z_lo).
Axes of the slice: x: 4, y: 8, z: 12 (z_hi: 2, z_lo: 6; z = z_hi * 6 + z_lo), core: 2. Of those that a mesh axis runs over, the one named last changes fastest.
Arguments:
- activations: bfloat16 [128, 32, 24, 256], P('dp', None, 'space'), may hold values from -6 to 6
- cotangent: bfloat16 [128, 128, 12, 64], P('dp', None, 'space'), may hold values from -12 to 12
- weight_mid: bfloat16 [3, 3, 3, 32, 64], replicated, may hold values from -0.21875 to 0.21875
- weight_deep: bfloat16 [3, 3, 3, 64, 128], replicated, may hold values from -0.15625 to 0.15625
Outputs:
- grad_input: bfloat16 [128, 32, 24, 256], P('dp', None, 'space')
- grad_mid: float32 [3, 3, 3, 32, 64], replicated
- grad_deep: float32 [3, 3, 3, 64, 128], replicated
The draws below stay inside these ranges and needn't reach their ends.
All inputs are finite; a program needn't handle non-finite values.
Results may differ from the reference program's by a relative error of at most 0.0059.
Values may be sent and summed in bfloat16 or wider, within the bound.
No kernel may reach another device: no remote copies, remote signals or barrier semaphores. Data moves between devices by JAX's collectives and lax.ppermute only.
A program may use at most 32 MiB of HBM per device.

```python
from functools import partial
import jax
import jax.numpy as jnp
from jax import lax

C1 = 32
C2 = 64
C3 = 128
ROWS = 4
COLS = 64
SAMPLES = 128
DEPTH = 24
PLANE = 256
PLANE3 = 64
DEPTH3 = 12


def shard_levels(own_key, shape, cuts, smallest, high):
    def one(axis_at, shards_of):
        draws = jax.random.uniform(jax.random.fold_in(jax.random.fold_in(own_key, 6), axis_at), (shards_of,), jnp.float32, smallest / len(cuts), high / len(cuts))
        return jnp.repeat(jnp.exp(draws), shape[axis_at] // shards_of).reshape((-1,) + (1,) * (len(shape) - axis_at - 1))

    gain = one(*cuts[0])
    for cut in cuts[1:]:
        gain = gain * one(*cut)
    return gain


def scatter_about(stream_key, shape, scale, reach, split=(), dtype=jnp.bfloat16):
    loudness = shard_levels(stream_key, shape, split, -0.22, 0.18) if split else 1.0
    values = jax.random.normal(stream_key, shape, jnp.float32) * scale * loudness
    return jnp.minimum(jnp.maximum(values, -reach), reach).astype(dtype)


def setup_inputs(seed: int = 0) -> dict:
    keys = jax.random.split(jax.random.key(seed), 5)
    activations = scatter_about(keys[0], (SAMPLES, C1, DEPTH, PLANE), 1.0, 6.0, ((0, 128), (2, 6)))
    cotangent = scatter_about(keys[1], (SAMPLES, C3, DEPTH3, PLANE3), 2.0, 12.0, ((0, 128), (2, 6)))
    weight_mid = scatter_about(keys[2], (3, 3, 3, C1, C2), (27 * C1) ** -0.5, 0.21875)
    weight_deep = scatter_about(keys[3], (3, 3, 3, C2, C3), (27 * C2) ** -0.5, 0.15625)
    return dict(activations=activations, cotangent=cotangent, weight_mid=weight_mid, weight_deep=weight_deep)


def conv_same(field, kernel):
    return lax.conv_general_dilated(field[None], kernel, (1, 1, 1), 'SAME', dimension_numbers=('NCDHW', 'DHWIO', 'NCDHW'), precision=lax.Precision.HIGHEST)[0]

def flip_taps(kernel):
    return jnp.transpose(kernel[::-1, ::-1, ::-1], (0, 1, 2, 4, 3))

def pool_cube(values):
    chans, depth_len, row_count, col_count = values.shape
    blocks = values.reshape(chans, depth_len // 2, 2, row_count // 2, 2, col_count // 2, 2)
    return lax.optimization_barrier(jnp.mean(blocks, axis=(2, 4, 6)))

def upsample_cube(values):
    spread = jnp.repeat(values, 2, axis=1)
    spread = jnp.repeat(spread, 2, axis=2)
    return jnp.repeat(spread, 2, axis=3)

def gelu_back(pre_values, upstream):
    return jax.vjp(partial(jax.nn.gelu, approximate=True), pre_values)[1](upstream)[0]

def weight_terms(field, grad_out, kernel):
    return jax.vjp(lambda kern: conv_same(field, kern), kernel)[1](grad_out)[0]

def one_sample(source, upstream, mid_kernel, deep_kernel):
    depth_len = source.shape[1]
    source_f = source.astype(jnp.float32).reshape(C1, depth_len, ROWS, COLS)
    pre_mid = conv_same(source_f, mid_kernel)
    pooled = pool_cube(jax.nn.gelu(pre_mid, approximate=True)).astype(jnp.bfloat16)
    pooled_f = lax.optimization_barrier(pooled).astype(jnp.float32)
    pre_deep = conv_same(pooled_f, deep_kernel)
    upstream_f = upstream.astype(jnp.float32).reshape(C3, depth_len // 2, ROWS // 2, COLS // 2)
    deep_grad = gelu_back(pre_deep, upstream_f).astype(jnp.bfloat16)
    deep_grad_f = lax.optimization_barrier(deep_grad).astype(jnp.float32)
    terms_deep = weight_terms(pooled_f, deep_grad_f, deep_kernel)
    back_pooled = conv_same(deep_grad_f, flip_taps(deep_kernel))
    spread = upsample_cube(back_pooled) * 0.125
    mid_grad = gelu_back(pre_mid, spread).astype(jnp.bfloat16)
    mid_grad_f = lax.optimization_barrier(mid_grad).astype(jnp.float32)
    terms_mid = weight_terms(source_f, mid_grad_f, mid_kernel)
    grad_in = conv_same(mid_grad_f, flip_taps(mid_kernel)).astype(jnp.bfloat16)
    return (grad_in.reshape(C1, depth_len, ROWS * COLS), terms_mid, terms_deep)

def reference(activations, cotangent, weight_mid, weight_deep):
    mid_kernel = weight_mid.astype(jnp.float32)
    deep_kernel = weight_deep.astype(jnp.float32)

    def advance(carry, inputs):
        grad_in, terms_mid, terms_deep = one_sample(inputs[0], inputs[1], mid_kernel, deep_kernel)
        return ((carry[0] + terms_mid, carry[1] + terms_deep), grad_in)
    start = (jnp.zeros(weight_mid.shape, jnp.float32), jnp.zeros(weight_deep.shape, jnp.float32))
    totals, grad_input = lax.scan(advance, start, (activations, cotangent))
    return (grad_input, totals[0] / SAMPLES, totals[1] / SAMPLES)
```

```python
import jax
import jax.numpy as jnp
from jax import lax
from jax.sharding import PartitionSpec as P

ROWS = 4
COLS = 64


def extended(block, sides, width):
    for axis, dim in sides:
        count = lax.axis_size(axis)
        forward = [(i, i + 1) for i in range(count - 1)]
        backward = [(target, source) for source, target in forward]
        low = lax.ppermute(
            lax.slice_in_dim(block, block.shape[dim] - width, None, axis=dim), axis, forward
        )
        high = lax.ppermute(lax.slice_in_dim(block, 0, width, axis=dim), axis, backward)
        block = jnp.concatenate([low, block, high], axis=dim)
    return block


def shifted(planes, row_step, col_step, row_count, col_count):
    margin = col_count + 1
    widened = jnp.pad(planes, ((0, 0), (0, 0), (margin, margin)))
    offset = margin + row_step * col_count + col_step
    moved_cells = widened[:, :, offset : offset + row_count * col_count]
    column = jnp.arange(row_count * col_count) % col_count + col_step
    inside = (column >= 0) & (column < col_count)
    return jnp.where(inside, moved_cells, jnp.zeros_like(moved_cells))


def tap_patches(padded, depth_tap, row_tap, row_count, col_count):
    depth_len = padded.shape[1] - 2
    planes = padded[:, depth_tap : depth_tap + depth_len]
    stacked = jnp.stack(
        [shifted(planes, row_tap - 1, col_tap - 1, row_count, col_count) for col_tap in range(3)]
    )
    return stacked.reshape(3 * planes.shape[0], depth_len * planes.shape[2])


def conv_cube(padded, kernel, row_count, col_count):
    depth_len = padded.shape[1] - 2
    chans_in = kernel.shape[3]
    chans_out = kernel.shape[4]
    summed = jnp.zeros((chans_out, depth_len * padded.shape[2]), jnp.float32)
    for depth_tap in range(3):
        for row_tap in range(3):
            patches = tap_patches(padded, depth_tap, row_tap, row_count, col_count)
            tap_block = kernel[depth_tap, row_tap].reshape(3 * chans_in, chans_out)
            summed = summed + lax.dot_general(
                tap_block, patches, (((0,), (0,)), ((), ())), preferred_element_type=jnp.float32
            )
    return summed.reshape(chans_out, depth_len, padded.shape[2])


def weight_terms(padded, grad_out, row_count, col_count):
    chans_in = padded.shape[0]
    chans_out = grad_out.shape[0]
    flat_grad = grad_out.reshape(chans_out, -1)
    pieces = []
    for depth_tap in range(3):
        for row_tap in range(3):
            patches = tap_patches(padded, depth_tap, row_tap, row_count, col_count)
            pieces.append(
                lax.dot_general(
                    patches, flat_grad, (((1,), (1,)), ((), ())), preferred_element_type=jnp.float32
                )
            )
    return jnp.stack(pieces).reshape(3, 3, 3, chans_in, chans_out)


def flip_taps(kernel):
    return jnp.transpose(kernel[::-1, ::-1, ::-1], (0, 1, 2, 4, 3))


def pool_matrix(row_count, col_count):
    cells = jnp.arange(row_count * col_count)
    target = cells // col_count // 2 * (col_count // 2) + cells % col_count // 2
    return (target[:, None] == jnp.arange(row_count * col_count // 4)[None, :]).astype(jnp.float32)


def pool_cube(values, matrix):
    chans, depth_len, plane_len = values.shape
    paired = values.reshape(chans, depth_len // 2, 2, plane_len).sum(axis=2)
    return jnp.einsum("cdp,pq->cdq", paired, matrix, precision=lax.Precision.HIGHEST) * 0.125


def upsample_cube(values, matrix):
    spread = jnp.einsum("cdq,pq->cdp", values, matrix, precision=lax.Precision.HIGHEST)
    return jnp.repeat(spread, 2, axis=1)


def gelu_fwd(values):
    return jax.nn.gelu(values, approximate=True)


def gelu_back(pre_values, upstream):
    return jax.vjp(gelu_fwd, pre_values)[1](upstream)[0]


def extend(field, width):
    return extended(field, (("space", 1),), width)


def mean_terms(terms, axes, samples):
    devices = 1
    for axis in axes:
        devices *= lax.axis_size(axis)
    flat = jnp.concatenate([term.reshape(-1) for term in terms])
    total = flat.shape[0]
    padded = -(-total // devices) * devices
    flat = jnp.pad(flat, (0, padded - total))
    pieces = lax.all_to_all(flat.reshape(devices, -1), axes, 0, 0, tiled=True)
    piece = pieces.sum(axis=0) / samples
    spread = jnp.broadcast_to(piece, (devices,) + piece.shape)
    gathered = lax.all_to_all(spread, axes, 0, 0, tiled=True).reshape(-1)[:total]
    results = []
    start = 0
    for term in terms:
        results.append(gathered[start : start + term.size].reshape(term.shape))
        start += term.size
    return tuple(results)


def shards(activations, cotangent, weight_mid, weight_deep):
    row_count = ROWS
    col_count = COLS
    source = activations[0]
    matrix = pool_matrix(row_count, col_count)
    source_ext = extend(source, 1)
    mid_pre = conv_cube(source_ext, weight_mid, row_count, col_count)
    pooled_ext = extend(pool_cube(gelu_fwd(mid_pre), matrix).astype(jnp.bfloat16), 1)
    deep_pre = conv_cube(pooled_ext, weight_deep, row_count // 2, col_count // 2)
    deep_grad = gelu_back(deep_pre, cotangent[0].astype(jnp.float32)).astype(jnp.bfloat16)
    deep_terms = weight_terms(pooled_ext, deep_grad, row_count // 2, col_count // 2)
    samples = lax.axis_size("dp")
    back_pooled = conv_cube(
        extend(deep_grad, 1), flip_taps(weight_deep), row_count // 2, col_count // 2
    )
    spread = upsample_cube(back_pooled, matrix) * 0.125
    mid_grad = gelu_back(mid_pre, spread).astype(jnp.bfloat16)
    mid_terms = weight_terms(source_ext, mid_grad, row_count, col_count)
    grad_input = conv_cube(extend(mid_grad, 1), flip_taps(weight_mid), row_count, col_count).astype(
        jnp.bfloat16
    )
    grad_mid, grad_deep = mean_terms((mid_terms, deep_terms), ("dp", "space"), samples)
    return (grad_input[None], grad_mid, grad_deep)


def solution(mesh):
    in_specs = (P("dp", None, "space", None), P("dp", None, "space", None), P(), P())
    out_specs = (P("dp", None, "space", None), P(), P())
    return jax.shard_map(shards, mesh=mesh, in_specs=in_specs, out_specs=out_specs, check_vma=False)
```

```python
import jax
import jax.numpy as jnp
from jax import lax
from jax.sharding import PartitionSpec as P

ROWS = 4
COLS = 64


def extended(block, sides, width):
    for axis, dim in sides:
        count = lax.axis_size(axis)
        forward = [(i, i + 1) for i in range(count - 1)]
        backward = [(target, source) for source, target in forward]
        low = lax.ppermute(
            lax.slice_in_dim(block, block.shape[dim] - width, None, axis=dim), axis, forward
        )
        high = lax.ppermute(lax.slice_in_dim(block, 0, width, axis=dim), axis, backward)
        block = jnp.concatenate([low, block, high], axis=dim)
    return block


def shifted(planes, row_step, col_step, row_count, col_count):
    margin = col_count + 1
    widened = jnp.pad(planes, ((0, 0), (0, 0), (margin, margin)))
    offset = margin + row_step * col_count + col_step
    moved_cells = widened[:, :, offset : offset + row_count * col_count]
    column = jnp.arange(row_count * col_count) % col_count + col_step
    inside = (column >= 0) & (column < col_count)
    return jnp.where(inside, moved_cells, jnp.zeros_like(moved_cells))


def tap_patches(padded, depth_tap, row_tap, row_count, col_count):
    depth_len = padded.shape[1] - 2
    planes = padded[:, depth_tap : depth_tap + depth_len]
    stacked = jnp.stack(
        [shifted(planes, row_tap - 1, col_tap - 1, row_count, col_count) for col_tap in range(3)]
    )
    return stacked.reshape(3 * planes.shape[0], depth_len * planes.shape[2])


def conv_cube(padded, kernel, row_count, col_count):
    depth_len = padded.shape[1] - 2
    chans_in = kernel.shape[3]
    chans_out = kernel.shape[4]
    summed = jnp.zeros((chans_out, depth_len * padded.shape[2]), jnp.float32)
    for depth_tap in range(3):
        for row_tap in range(3):
            patches = tap_patches(padded, depth_tap, row_tap, row_count, col_count)
            tap_block = kernel[depth_tap, row_tap].reshape(3 * chans_in, chans_out)
            summed = summed + lax.dot_general(
                tap_block, patches, (((0,), (0,)), ((), ())), preferred_element_type=jnp.float32
            )
    return summed.reshape(chans_out, depth_len, padded.shape[2])


def weight_terms(padded, grad_out, row_count, col_count):
    chans_in = padded.shape[0]
    chans_out = grad_out.shape[0]
    flat_grad = grad_out.reshape(chans_out, -1)
    pieces = []
    for depth_tap in range(3):
        for row_tap in range(3):
            patches = tap_patches(padded, depth_tap, row_tap, row_count, col_count)
            pieces.append(
                lax.dot_general(
                    patches, flat_grad, (((1,), (1,)), ((), ())), preferred_element_type=jnp.float32
                )
            )
    return jnp.stack(pieces).reshape(3, 3, 3, chans_in, chans_out)


def flip_taps(kernel):
    return jnp.transpose(kernel[::-1, ::-1, ::-1], (0, 1, 2, 4, 3))


def pool_matrix(row_count, col_count):
    cells = jnp.arange(row_count * col_count)
    target = cells // col_count // 2 * (col_count // 2) + cells % col_count // 2
    return (target[:, None] == jnp.arange(row_count * col_count // 4)[None, :]).astype(jnp.float32)


def pool_cube(values, matrix):
    chans, depth_len, plane_len = values.shape
    paired = values.reshape(chans, depth_len // 2, 2, plane_len).sum(axis=2)
    return jnp.einsum("cdp,pq->cdq", paired, matrix, precision=lax.Precision.HIGHEST) * 0.125


def upsample_cube(values, matrix):
    spread = jnp.einsum("cdq,pq->cdp", values, matrix, precision=lax.Precision.HIGHEST)
    return jnp.repeat(spread, 2, axis=1)


def gelu_fwd(values):
    return jax.nn.gelu(values, approximate=True)


def gelu_back(pre_values, upstream):
    return jax.vjp(gelu_fwd, pre_values)[1](upstream)[0]


def extend(field, width):
    return extended(field, (("space", 1),), width)


def mean_terms(terms, axes, samples):
    devices = 1
    for axis in axes:
        devices *= lax.axis_size(axis)
    flat = jnp.concatenate([term.reshape(-1) for term in terms])
    total = flat.shape[0]
    padded = -(-total // devices) * devices
    flat = jnp.pad(flat, (0, padded - total))
    pieces = lax.all_to_all(flat.reshape(devices, -1), axes, 0, 0, tiled=True)
    piece = pieces.sum(axis=0) / samples
    spread = jnp.broadcast_to(piece.astype(jnp.bfloat16), (devices,) + piece.shape)
    gathered = lax.all_to_all(spread, axes, 0, 0, tiled=True).reshape(-1)[:total]
    gathered = gathered.astype(jnp.float32)
    results = []
    start = 0
    for term in terms:
        results.append(gathered[start : start + term.size].reshape(term.shape))
        start += term.size
    return tuple(results)


def shards(activations, cotangent, weight_mid, weight_deep):
    row_count = ROWS
    col_count = COLS
    source = activations[0]
    matrix = pool_matrix(row_count, col_count)
    source_ext = extend(source, 1)
    mid_pre = conv_cube(source_ext, weight_mid, row_count, col_count)
    pooled_ext = extend(pool_cube(gelu_fwd(mid_pre), matrix).astype(jnp.bfloat16), 1)
    deep_pre = conv_cube(pooled_ext, weight_deep, row_count // 2, col_count // 2)
    deep_grad = gelu_back(deep_pre, cotangent[0].astype(jnp.float32)).astype(jnp.bfloat16)
    deep_terms = weight_terms(pooled_ext, deep_grad, row_count // 2, col_count // 2)
    samples = lax.axis_size("dp")
    back_pooled = conv_cube(
        extend(deep_grad, 1), flip_taps(weight_deep), row_count // 2, col_count // 2
    )
    spread = upsample_cube(back_pooled, matrix) * 0.125
    mid_grad = gelu_back(mid_pre, spread).astype(jnp.bfloat16)
    mid_terms = weight_terms(source_ext, mid_grad, row_count, col_count)
    grad_input = conv_cube(extend(mid_grad, 1), flip_taps(weight_mid), row_count, col_count).astype(
        jnp.bfloat16
    )
    grad_mid, grad_deep = mean_terms((mid_terms, deep_terms), ("dp", "space"), samples)
    return (grad_input[None], grad_mid, grad_deep)


def solution(mesh):
    in_specs = (P("dp", None, "space", None), P("dp", None, "space", None), P(), P())
    out_specs = (P("dp", None, "space", None), P(), P())
    return jax.shard_map(shards, mesh=mesh, in_specs=in_specs, out_specs=out_specs, check_vma=False)
```

```python
import jax
import jax.numpy as jnp
from jax import lax
from jax.sharding import Mesh, PartitionSpec as P

ROWS = 4
COLS = 64


def extended(block, sides, width):
    for axis, dim in sides:
        count = lax.axis_size(axis)
        forward = [(i, i + 1) for i in range(count - 1)]
        backward = [(target, source) for source, target in forward]
        low = lax.ppermute(
            lax.slice_in_dim(block, block.shape[dim] - width, None, axis=dim), axis, forward
        )
        high = lax.ppermute(lax.slice_in_dim(block, 0, width, axis=dim), axis, backward)
        block = jnp.concatenate([low, block, high], axis=dim)
    return block


def shifted(planes, row_step, col_step, row_count, col_count):
    margin = col_count + 1
    widened = jnp.pad(planes, ((0, 0), (0, 0), (margin, margin)))
    offset = margin + row_step * col_count + col_step
    moved_cells = widened[:, :, offset : offset + row_count * col_count]
    column = jnp.arange(row_count * col_count) % col_count + col_step
    inside = (column >= 0) & (column < col_count)
    return jnp.where(inside, moved_cells, jnp.zeros_like(moved_cells))


def tap_patches(padded, depth_tap, row_tap, row_count, col_count):
    depth_len = padded.shape[1] - 2
    planes = padded[:, depth_tap : depth_tap + depth_len]
    stacked = jnp.stack(
        [shifted(planes, row_tap - 1, col_tap - 1, row_count, col_count) for col_tap in range(3)]
    )
    return stacked.reshape(3 * planes.shape[0], depth_len * planes.shape[2])


def conv_cube(padded, kernel, row_count, col_count):
    depth_len = padded.shape[1] - 2
    chans_in = kernel.shape[3]
    chans_out = kernel.shape[4]
    summed = jnp.zeros((chans_out, depth_len * padded.shape[2]), jnp.float32)
    for depth_tap in range(3):
        for row_tap in range(3):
            patches = tap_patches(padded, depth_tap, row_tap, row_count, col_count)
            tap_block = kernel[depth_tap, row_tap].reshape(3 * chans_in, chans_out)
            summed = summed + lax.dot_general(
                tap_block, patches, (((0,), (0,)), ((), ())), preferred_element_type=jnp.float32
            )
    return summed.reshape(chans_out, depth_len, padded.shape[2])


def weight_terms(padded, grad_out, row_count, col_count):
    chans_in = padded.shape[0]
    chans_out = grad_out.shape[0]
    flat_grad = grad_out.reshape(chans_out, -1)
    pieces = []
    for depth_tap in range(3):
        for row_tap in range(3):
            patches = tap_patches(padded, depth_tap, row_tap, row_count, col_count)
            pieces.append(
                lax.dot_general(
                    patches, flat_grad, (((1,), (1,)), ((), ())), preferred_element_type=jnp.float32
                )
            )
    return jnp.stack(pieces).reshape(3, 3, 3, chans_in, chans_out)


def flip_taps(kernel):
    return jnp.transpose(kernel[::-1, ::-1, ::-1], (0, 1, 2, 4, 3))


def pool_matrix(row_count, col_count):
    cells = jnp.arange(row_count * col_count)
    target = cells // col_count // 2 * (col_count // 2) + cells % col_count // 2
    return (target[:, None] == jnp.arange(row_count * col_count // 4)[None, :]).astype(jnp.float32)


def pool_cube(values, matrix):
    chans, depth_len, plane_len = values.shape
    paired = values.reshape(chans, depth_len // 2, 2, plane_len).sum(axis=2)
    return jnp.einsum("cdp,pq->cdq", paired, matrix, precision=lax.Precision.HIGHEST) * 0.125


def upsample_cube(values, matrix):
    spread = jnp.einsum("cdq,pq->cdp", values, matrix, precision=lax.Precision.HIGHEST)
    return jnp.repeat(spread, 2, axis=1)


def gelu_fwd(values):
    return jax.nn.gelu(values, approximate=True)


def gelu_back(pre_values, upstream):
    return jax.vjp(gelu_fwd, pre_values)[1](upstream)[0]


def extend(field, width):
    return extended(field, (("space", 1),), width)


def mean_terms(terms, samples):
    axes = ("chips", "space")
    devices = lax.axis_size("chips") * lax.axis_size("space")
    flat = jnp.concatenate([term.reshape(-1) for term in terms])
    total = flat.shape[0]
    padded = -(-total // (2 * devices)) * 2 * devices
    halves = jnp.pad(flat, (0, padded - total)).reshape(2, -1)
    core = lax.axis_index("core")
    swap = [(0, 1), (1, 0)]
    own = lax.dynamic_index_in_dim(halves, core, 0, keepdims=False)
    other = lax.dynamic_index_in_dim(halves, 1 - core, 0, keepdims=False)
    own = own + lax.ppermute(other, "core", swap)
    pieces = lax.all_to_all(own.reshape(devices, -1), axes, 0, 0, tiled=True)
    piece = (pieces.sum(axis=0) / samples).astype(jnp.bfloat16)
    spread = jnp.broadcast_to(piece, (devices,) + piece.shape)
    mine = lax.all_to_all(spread, axes, 0, 0, tiled=True).reshape(-1)
    theirs = lax.ppermute(mine, "core", swap)
    first = jnp.where(core == 0, mine, theirs)
    second = jnp.where(core == 0, theirs, mine)
    gathered = jnp.concatenate([first, second])[:total].astype(jnp.float32)
    results = []
    start = 0
    for term in terms:
        results.append(gathered[start : start + term.size].reshape(term.shape))
        start += term.size
    return tuple(results)


def shards(activations, cotangent, weight_mid, weight_deep):
    row_count = ROWS
    col_count = COLS
    source = activations[0]
    matrix = pool_matrix(row_count, col_count)
    source_ext = extend(source, 1)
    mid_pre = conv_cube(source_ext, weight_mid, row_count, col_count)
    pooled_ext = extend(pool_cube(gelu_fwd(mid_pre), matrix).astype(jnp.bfloat16), 1)
    deep_pre = conv_cube(pooled_ext, weight_deep, row_count // 2, col_count // 2)
    deep_grad = gelu_back(deep_pre, cotangent[0].astype(jnp.float32)).astype(jnp.bfloat16)
    deep_terms = weight_terms(pooled_ext, deep_grad, row_count // 2, col_count // 2)
    samples = lax.axis_size("chips") * lax.axis_size("core")
    back_pooled = conv_cube(
        extend(deep_grad, 1), flip_taps(weight_deep), row_count // 2, col_count // 2
    )
    spread = upsample_cube(back_pooled, matrix) * 0.125
    mid_grad = gelu_back(mid_pre, spread).astype(jnp.bfloat16)
    mid_terms = weight_terms(source_ext, mid_grad, row_count, col_count)
    grad_input = conv_cube(extend(mid_grad, 1), flip_taps(weight_mid), row_count, col_count).astype(
        jnp.bfloat16
    )
    grad_mid, grad_deep = mean_terms((mid_terms, deep_terms), samples)
    return (grad_input[None], grad_mid, grad_deep)


def solution(mesh):
    samples, slabs = mesh.devices.shape
    pairs = Mesh(mesh.devices.reshape(samples // 2, 2, slabs), ("chips", "core", "space"))
    in_specs = (
        P(("chips", "core"), None, "space", None),
        P(("chips", "core"), None, "space", None),
        P(),
        P(),
    )
    out_specs = (P(("chips", "core"), None, "space", None), P(), P())
    return jax.shard_map(shards, mesh=pairs, in_specs=in_specs, out_specs=out_specs, check_vma=False)
```

```python
import jax
import jax.numpy as jnp
from jax import lax
from jax.sharding import Mesh, PartitionSpec as P

ROWS = 4
COLS = 64


def extended(block, sides, width):
    for axis, dim in sides:
        count = lax.axis_size(axis)
        forward = [(i, i + 1) for i in range(count - 1)]
        backward = [(target, source) for source, target in forward]
        low = lax.ppermute(
            lax.slice_in_dim(block, block.shape[dim] - width, None, axis=dim), axis, forward
        )
        high = lax.ppermute(lax.slice_in_dim(block, 0, width, axis=dim), axis, backward)
        block = jnp.concatenate([low, block, high], axis=dim)
    return block


def shifted(planes, row_step, col_step, row_count, col_count):
    margin = col_count + 1
    widened = jnp.pad(planes, ((0, 0), (0, 0), (margin, margin)))
    offset = margin + row_step * col_count + col_step
    moved_cells = widened[:, :, offset : offset + row_count * col_count]
    column = jnp.arange(row_count * col_count) % col_count + col_step
    inside = (column >= 0) & (column < col_count)
    return jnp.where(inside, moved_cells, jnp.zeros_like(moved_cells))


def tap_patches(padded, depth_tap, row_tap, row_count, col_count):
    depth_len = padded.shape[1] - 2
    planes = padded[:, depth_tap : depth_tap + depth_len]
    stacked = jnp.stack(
        [shifted(planes, row_tap - 1, col_tap - 1, row_count, col_count) for col_tap in range(3)]
    )
    return stacked.reshape(3 * planes.shape[0], depth_len * planes.shape[2])


def conv_cube(padded, kernel, row_count, col_count):
    depth_len = padded.shape[1] - 2
    chans_in = kernel.shape[3]
    chans_out = kernel.shape[4]
    summed = jnp.zeros((chans_out, depth_len * padded.shape[2]), jnp.float32)
    for depth_tap in range(3):
        for row_tap in range(3):
            patches = tap_patches(padded, depth_tap, row_tap, row_count, col_count)
            tap_block = kernel[depth_tap, row_tap].reshape(3 * chans_in, chans_out)
            summed = summed + lax.dot_general(
                tap_block, patches, (((0,), (0,)), ((), ())), preferred_element_type=jnp.float32
            )
    return summed.reshape(chans_out, depth_len, padded.shape[2])


def weight_terms(padded, grad_out, row_count, col_count):
    chans_in = padded.shape[0]
    chans_out = grad_out.shape[0]
    flat_grad = grad_out.reshape(chans_out, -1)
    pieces = []
    for depth_tap in range(3):
        for row_tap in range(3):
            patches = tap_patches(padded, depth_tap, row_tap, row_count, col_count)
            pieces.append(
                lax.dot_general(
                    patches, flat_grad, (((1,), (1,)), ((), ())), preferred_element_type=jnp.float32
                )
            )
    return jnp.stack(pieces).reshape(3, 3, 3, chans_in, chans_out)


def flip_taps(kernel):
    return jnp.transpose(kernel[::-1, ::-1, ::-1], (0, 1, 2, 4, 3))


def pool_matrix(row_count, col_count):
    cells = jnp.arange(row_count * col_count)
    target = cells // col_count // 2 * (col_count // 2) + cells % col_count // 2
    return (target[:, None] == jnp.arange(row_count * col_count // 4)[None, :]).astype(jnp.float32)


def pool_cube(values, matrix):
    chans, depth_len, plane_len = values.shape
    paired = values.reshape(chans, depth_len // 2, 2, plane_len).sum(axis=2)
    return jnp.einsum("cdp,pq->cdq", paired, matrix, precision=lax.Precision.HIGHEST) * 0.125


def upsample_cube(values, matrix):
    spread = jnp.einsum("cdq,pq->cdp", values, matrix, precision=lax.Precision.HIGHEST)
    return jnp.repeat(spread, 2, axis=1)


def gelu_fwd(values):
    return jax.nn.gelu(values, approximate=True)


def gelu_back(pre_values, upstream):
    return jax.vjp(gelu_fwd, pre_values)[1](upstream)[0]


def extend(field, width):
    return extended(field, (("space", 1),), width)


def swap_add(parts, axis):
    me = lax.axis_index(axis)
    halves = parts.reshape(2, -1)
    own = lax.dynamic_index_in_dim(halves, me, 0, keepdims=False)
    other = lax.dynamic_index_in_dim(halves, 1 - me, 0, keepdims=False)
    return own + lax.ppermute(other, axis, [(0, 1), (1, 0)])


def swap_join(part, axis):
    me = lax.axis_index(axis)
    theirs = lax.ppermute(part, axis, [(0, 1), (1, 0)])
    first = jnp.where(me == 0, part, theirs)
    second = jnp.where(me == 0, theirs, part)
    return jnp.concatenate([first, second])


def mean_terms(terms, samples):
    axes = ("rows", "z_high", "space")
    devices = lax.axis_size("rows") * lax.axis_size("z_high") * lax.axis_size("space")
    flat = jnp.concatenate([term.reshape(-1) for term in terms])
    total = flat.shape[0]
    padded = -(-total // (4 * devices)) * 4 * devices
    own = swap_add(jnp.pad(flat, (0, padded - total)), "core")
    own = swap_add(own, "x_low")
    pieces = lax.all_to_all(own.reshape(devices, -1), axes, 0, 0, tiled=True)
    piece = (pieces.sum(axis=0) / samples).astype(jnp.bfloat16)
    spread = jnp.broadcast_to(piece, (devices,) + piece.shape)
    mine = lax.all_to_all(spread, axes, 0, 0, tiled=True).reshape(-1)
    gathered = swap_join(swap_join(mine, "x_low"), "core")[:total].astype(jnp.float32)
    results = []
    start = 0
    for term in terms:
        results.append(gathered[start : start + term.size].reshape(term.shape))
        start += term.size
    return tuple(results)


def shards(activations, cotangent, weight_mid, weight_deep):
    row_count = ROWS
    col_count = COLS
    source = activations[0]
    matrix = pool_matrix(row_count, col_count)
    source_ext = extend(source, 1)
    mid_pre = conv_cube(source_ext, weight_mid, row_count, col_count)
    pooled_ext = extend(pool_cube(gelu_fwd(mid_pre), matrix).astype(jnp.bfloat16), 1)
    deep_pre = conv_cube(pooled_ext, weight_deep, row_count // 2, col_count // 2)
    deep_grad = gelu_back(deep_pre, cotangent[0].astype(jnp.float32)).astype(jnp.bfloat16)
    deep_terms = weight_terms(pooled_ext, deep_grad, row_count // 2, col_count // 2)
    samples = 1
    for axis in SAMPLE_AXES:
        samples *= lax.axis_size(axis)
    back_pooled = conv_cube(
        extend(deep_grad, 1), flip_taps(weight_deep), row_count // 2, col_count // 2
    )
    spread = upsample_cube(back_pooled, matrix) * 0.125
    mid_grad = gelu_back(mid_pre, spread).astype(jnp.bfloat16)
    mid_terms = weight_terms(source_ext, mid_grad, row_count, col_count)
    grad_input = conv_cube(extend(mid_grad, 1), flip_taps(weight_mid), row_count, col_count).astype(
        jnp.bfloat16
    )
    grad_mid, grad_deep = mean_terms((mid_terms, deep_terms), samples)
    return (grad_input[None], grad_mid, grad_deep)


SAMPLE_AXES = ("rows", "x_low", "z_high", "core")


def solution(mesh):
    samples, slabs = mesh.devices.shape
    split = Mesh(mesh.devices.reshape(samples // 8, 2, 2, 2, slabs), SAMPLE_AXES + ("space",))
    in_specs = (P(SAMPLE_AXES, None, "space", None), P(SAMPLE_AXES, None, "space", None), P(), P())
    out_specs = (P(SAMPLE_AXES, None, "space", None), P(), P())
    return jax.shard_map(shards, mesh=split, in_specs=in_specs, out_specs=out_specs, check_vma=False)
```

```python
import jax
import jax.numpy as jnp
from jax import lax
from jax.sharding import Mesh, PartitionSpec as P

ROWS = 4
COLS = 64


def extended(block, sides, width):
    for axis, dim in sides:
        count = lax.axis_size(axis)
        forward = [(i, i + 1) for i in range(count - 1)]
        backward = [(target, source) for source, target in forward]
        low = lax.ppermute(
            lax.slice_in_dim(block, block.shape[dim] - width, None, axis=dim), axis, forward
        )
        high = lax.ppermute(lax.slice_in_dim(block, 0, width, axis=dim), axis, backward)
        block = jnp.concatenate([low, block, high], axis=dim)
    return block


def shifted(planes, row_step, col_step, row_count, col_count):
    margin = col_count + 1
    widened = jnp.pad(planes, ((0, 0), (0, 0), (margin, margin)))
    offset = margin + row_step * col_count + col_step
    moved_cells = widened[:, :, offset : offset + row_count * col_count]
    column = jnp.arange(row_count * col_count) % col_count + col_step
    inside = (column >= 0) & (column < col_count)
    return jnp.where(inside, moved_cells, jnp.zeros_like(moved_cells))


def tap_patches(padded, depth_tap, row_tap, row_count, col_count):
    depth_len = padded.shape[1] - 2
    planes = padded[:, depth_tap : depth_tap + depth_len]
    stacked = jnp.stack(
        [shifted(planes, row_tap - 1, col_tap - 1, row_count, col_count) for col_tap in range(3)]
    )
    return stacked.reshape(3 * planes.shape[0], depth_len * planes.shape[2])


def conv_cube(padded, kernel, row_count, col_count):
    depth_len = padded.shape[1] - 2
    chans_in = kernel.shape[3]
    chans_out = kernel.shape[4]
    summed = jnp.zeros((chans_out, depth_len * padded.shape[2]), jnp.float32)
    for depth_tap in range(3):
        for row_tap in range(3):
            patches = tap_patches(padded, depth_tap, row_tap, row_count, col_count)
            tap_block = kernel[depth_tap, row_tap].reshape(3 * chans_in, chans_out)
            summed = summed + lax.dot_general(
                tap_block, patches, (((0,), (0,)), ((), ())), preferred_element_type=jnp.float32
            )
    return summed.reshape(chans_out, depth_len, padded.shape[2])


def weight_terms(padded, grad_out, row_count, col_count):
    chans_in = padded.shape[0]
    chans_out = grad_out.shape[0]
    flat_grad = grad_out.reshape(chans_out, -1)
    pieces = []
    for depth_tap in range(3):
        for row_tap in range(3):
            patches = tap_patches(padded, depth_tap, row_tap, row_count, col_count)
            pieces.append(
                lax.dot_general(
                    patches, flat_grad, (((1,), (1,)), ((), ())), preferred_element_type=jnp.float32
                )
            )
    return jnp.stack(pieces).reshape(3, 3, 3, chans_in, chans_out)


def flip_taps(kernel):
    return jnp.transpose(kernel[::-1, ::-1, ::-1], (0, 1, 2, 4, 3))


def pool_matrix(row_count, col_count):
    cells = jnp.arange(row_count * col_count)
    target = cells // col_count // 2 * (col_count // 2) + cells % col_count // 2
    return (target[:, None] == jnp.arange(row_count * col_count // 4)[None, :]).astype(jnp.float32)


def pool_cube(values, matrix):
    chans, depth_len, plane_len = values.shape
    paired = values.reshape(chans, depth_len // 2, 2, plane_len).sum(axis=2)
    return jnp.einsum("cdp,pq->cdq", paired, matrix, precision=lax.Precision.HIGHEST) * 0.125


def upsample_cube(values, matrix):
    spread = jnp.einsum("cdq,pq->cdp", values, matrix, precision=lax.Precision.HIGHEST)
    return jnp.repeat(spread, 2, axis=1)


def gelu_fwd(values):
    return jax.nn.gelu(values, approximate=True)


def gelu_back(pre_values, upstream):
    return jax.vjp(gelu_fwd, pre_values)[1](upstream)[0]


def extend(field, width):
    return extended(field, (("space", 1),), width)


def swap_add(parts, axis):
    me = lax.axis_index(axis)
    halves = parts.reshape(2, -1)
    own = lax.dynamic_index_in_dim(halves, me, 0, keepdims=False)
    other = lax.dynamic_index_in_dim(halves, 1 - me, 0, keepdims=False)
    return own + lax.ppermute(other, axis, [(0, 1), (1, 0)])


def swap_join(part, axis):
    me = lax.axis_index(axis)
    theirs = lax.ppermute(part, axis, [(0, 1), (1, 0)])
    first = jnp.where(me == 0, part, theirs)
    second = jnp.where(me == 0, theirs, part)
    return jnp.concatenate([first, second])


def mean_terms(terms, samples):
    axes = ("y_high", "x_high", "z_high", "space")
    devices = 1
    for axis in axes:
        devices *= lax.axis_size(axis)
    flat = jnp.concatenate([term.reshape(-1) for term in terms])
    total = flat.shape[0]
    padded = -(-total // (8 * devices)) * 8 * devices
    own = swap_add(jnp.pad(flat, (0, padded - total)), "core")
    own = swap_add(own, "x_low")
    own = swap_add(own, "y_low")
    pieces = lax.all_to_all(own.reshape(devices, -1), axes, 0, 0, tiled=True)
    piece = (pieces.sum(axis=0) / samples).astype(jnp.bfloat16)
    spread = jnp.broadcast_to(piece, (devices,) + piece.shape)
    mine = lax.all_to_all(spread, axes, 0, 0, tiled=True).reshape(-1)
    gathered = swap_join(swap_join(swap_join(mine, "y_low"), "x_low"), "core")[:total].astype(jnp.float32)
    results = []
    start = 0
    for term in terms:
        results.append(gathered[start : start + term.size].reshape(term.shape))
        start += term.size
    return tuple(results)


def shards(activations, cotangent, weight_mid, weight_deep):
    row_count = ROWS
    col_count = COLS
    source = activations[0]
    matrix = pool_matrix(row_count, col_count)
    source_ext = extend(source, 1)
    mid_pre = conv_cube(source_ext, weight_mid, row_count, col_count)
    pooled_ext = extend(pool_cube(gelu_fwd(mid_pre), matrix).astype(jnp.bfloat16), 1)
    deep_pre = conv_cube(pooled_ext, weight_deep, row_count // 2, col_count // 2)
    deep_grad = gelu_back(deep_pre, cotangent[0].astype(jnp.float32)).astype(jnp.bfloat16)
    deep_terms = weight_terms(pooled_ext, deep_grad, row_count // 2, col_count // 2)
    samples = 1
    for axis in SAMPLE_AXES:
        samples *= lax.axis_size(axis)
    back_pooled = conv_cube(
        extend(deep_grad, 1), flip_taps(weight_deep), row_count // 2, col_count // 2
    )
    spread = upsample_cube(back_pooled, matrix) * 0.125
    mid_grad = gelu_back(mid_pre, spread).astype(jnp.bfloat16)
    mid_terms = weight_terms(source_ext, mid_grad, row_count, col_count)
    grad_input = conv_cube(extend(mid_grad, 1), flip_taps(weight_mid), row_count, col_count).astype(
        jnp.bfloat16
    )
    grad_mid, grad_deep = mean_terms((mid_terms, deep_terms), samples)
    return (grad_input[None], grad_mid, grad_deep)


SAMPLE_AXES = ("y_high", "y_low", "x_high", "x_low", "z_high", "core")


def solution(mesh):
    samples, slabs = mesh.devices.shape
    split = Mesh(mesh.devices.reshape(samples // 32, 2, 2, 2, 2, 2, slabs), SAMPLE_AXES + ("space",))
    in_specs = (P(SAMPLE_AXES, None, "space", None), P(SAMPLE_AXES, None, "space", None), P(), P())
    out_specs = (P(SAMPLE_AXES, None, "space", None), P(), P())
    return jax.shard_map(shards, mesh=split, in_specs=in_specs, out_specs=out_specs, check_vma=False)
```

```python
import jax
import jax.numpy as jnp
from jax import lax
from jax.sharding import Mesh, PartitionSpec as P

ROWS = 4
COLS = 64


def extended(block, sides, width):
    for axis, dim in sides:
        count = lax.axis_size(axis)
        forward = [(i, i + 1) for i in range(count - 1)]
        backward = [(target, source) for source, target in forward]
        low = lax.ppermute(
            lax.slice_in_dim(block, block.shape[dim] - width, None, axis=dim), axis, forward
        )
        high = lax.ppermute(lax.slice_in_dim(block, 0, width, axis=dim), axis, backward)
        block = jnp.concatenate([low, block, high], axis=dim)
    return block


def shifted(planes, row_step, col_step, row_count, col_count):
    margin = col_count + 1
    widened = jnp.pad(planes, ((0, 0), (0, 0), (margin, margin)))
    offset = margin + row_step * col_count + col_step
    moved_cells = widened[:, :, offset : offset + row_count * col_count]
    column = jnp.arange(row_count * col_count) % col_count + col_step
    inside = (column >= 0) & (column < col_count)
    return jnp.where(inside, moved_cells, jnp.zeros_like(moved_cells))


def tap_patches(padded, depth_tap, row_tap, row_count, col_count):
    depth_len = padded.shape[1] - 2
    planes = padded[:, depth_tap : depth_tap + depth_len]
    stacked = jnp.stack(
        [shifted(planes, row_tap - 1, col_tap - 1, row_count, col_count) for col_tap in range(3)]
    )
    return stacked.reshape(3 * planes.shape[0], depth_len * planes.shape[2])


def conv_cube(padded, kernel, row_count, col_count):
    depth_len = padded.shape[1] - 2
    chans_in = kernel.shape[3]
    chans_out = kernel.shape[4]
    summed = jnp.zeros((chans_out, depth_len * padded.shape[2]), jnp.float32)
    for depth_tap in range(3):
        for row_tap in range(3):
            patches = tap_patches(padded, depth_tap, row_tap, row_count, col_count)
            tap_block = kernel[depth_tap, row_tap].reshape(3 * chans_in, chans_out)
            summed = summed + lax.dot_general(
                tap_block, patches, (((0,), (0,)), ((), ())), preferred_element_type=jnp.float32
            )
    return summed.reshape(chans_out, depth_len, padded.shape[2])


def weight_terms(padded, grad_out, row_count, col_count):
    chans_in = padded.shape[0]
    chans_out = grad_out.shape[0]
    flat_grad = grad_out.reshape(chans_out, -1)
    pieces = []
    for depth_tap in range(3):
        for row_tap in range(3):
            patches = tap_patches(padded, depth_tap, row_tap, row_count, col_count)
            pieces.append(
                lax.dot_general(
                    patches, flat_grad, (((1,), (1,)), ((), ())), preferred_element_type=jnp.float32
                )
            )
    return jnp.stack(pieces).reshape(3, 3, 3, chans_in, chans_out)


def flip_taps(kernel):
    return jnp.transpose(kernel[::-1, ::-1, ::-1], (0, 1, 2, 4, 3))


def pool_matrix(row_count, col_count):
    cells = jnp.arange(row_count * col_count)
    target = cells // col_count // 2 * (col_count // 2) + cells % col_count // 2
    return (target[:, None] == jnp.arange(row_count * col_count // 4)[None, :]).astype(jnp.float32)


def pool_cube(values, matrix):
    chans, depth_len, plane_len = values.shape
    paired = values.reshape(chans, depth_len // 2, 2, plane_len).sum(axis=2)
    return jnp.einsum("cdp,pq->cdq", paired, matrix, precision=lax.Precision.HIGHEST) * 0.125


def upsample_cube(values, matrix):
    spread = jnp.einsum("cdq,pq->cdp", values, matrix, precision=lax.Precision.HIGHEST)
    return jnp.repeat(spread, 2, axis=1)


def gelu_fwd(values):
    return jax.nn.gelu(values, approximate=True)


def gelu_back(pre_values, upstream):
    return jax.vjp(gelu_fwd, pre_values)[1](upstream)[0]


def extend(field, width):
    return extended(field, (("space", 1),), width)


def swap_add(parts, axis):
    me = lax.axis_index(axis)
    halves = parts.reshape(2, -1)
    own = lax.dynamic_index_in_dim(halves, me, 0, keepdims=False)
    other = lax.dynamic_index_in_dim(halves, 1 - me, 0, keepdims=False)
    return own + lax.ppermute(other, axis, [(0, 1), (1, 0)])


def swap_join(part, axis):
    me = lax.axis_index(axis)
    theirs = lax.ppermute(part, axis, [(0, 1), (1, 0)])
    first = jnp.where(me == 0, part, theirs)
    second = jnp.where(me == 0, theirs, part)
    return jnp.concatenate([first, second])


def mean_terms(terms, samples, rider):
    axes = ("rows", "z_high", "space")
    devices = lax.axis_size("rows") * lax.axis_size("z_high") * lax.axis_size("space")
    flat = jnp.concatenate([term.reshape(-1) for term in terms])
    total = flat.shape[0]
    padded = -(-total // (4 * devices)) * 4 * devices
    own = swap_add(jnp.pad(flat, (0, padded - total)), "core")
    own = swap_add(own, "x_low")
    own, rider = lax.optimization_barrier((own, rider))
    pieces = lax.all_to_all(own.reshape(devices, -1), axes, 0, 0, tiled=True)
    piece = (pieces.sum(axis=0) / samples).astype(jnp.bfloat16)
    spread = jnp.broadcast_to(piece, (devices,) + piece.shape)
    mine = lax.all_to_all(spread, axes, 0, 0, tiled=True).reshape(-1)
    gathered = swap_join(swap_join(mine, "x_low"), "core")[:total].astype(jnp.float32)
    results = []
    start = 0
    for term in terms:
        results.append(gathered[start : start + term.size].reshape(term.shape))
        start += term.size
    return tuple(results), rider


def shards(activations, cotangent, weight_mid, weight_deep):
    row_count = ROWS
    col_count = COLS
    source = activations[0]
    matrix = pool_matrix(row_count, col_count)
    source_ext = extend(source, 1)
    mid_pre = conv_cube(source_ext, weight_mid, row_count, col_count)
    pooled_ext = extend(pool_cube(gelu_fwd(mid_pre), matrix).astype(jnp.bfloat16), 1)
    deep_pre = conv_cube(pooled_ext, weight_deep, row_count // 2, col_count // 2)
    deep_grad = gelu_back(deep_pre, cotangent[0].astype(jnp.float32)).astype(jnp.bfloat16)
    deep_terms = weight_terms(pooled_ext, deep_grad, row_count // 2, col_count // 2)
    samples = 1
    for axis in SAMPLE_AXES:
        samples *= lax.axis_size(axis)
    back_pooled = conv_cube(
        extend(deep_grad, 1), flip_taps(weight_deep), row_count // 2, col_count // 2
    )
    spread = upsample_cube(back_pooled, matrix) * 0.125
    mid_grad = gelu_back(mid_pre, spread).astype(jnp.bfloat16)
    mid_terms = weight_terms(source_ext, mid_grad, row_count, col_count)
    (grad_mid, grad_deep), mid_grad = mean_terms((mid_terms, deep_terms), samples, mid_grad)
    grad_input = conv_cube(extend(mid_grad, 1), flip_taps(weight_mid), row_count, col_count).astype(
        jnp.bfloat16
    )
    return (grad_input[None], grad_mid, grad_deep)


SAMPLE_AXES = ("rows", "x_low", "z_high", "core")


def solution(mesh):
    samples, slabs = mesh.devices.shape
    split = Mesh(mesh.devices.reshape(samples // 8, 2, 2, 2, slabs), SAMPLE_AXES + ("space",))
    in_specs = (P(SAMPLE_AXES, None, "space", None), P(SAMPLE_AXES, None, "space", None), P(), P())
    out_specs = (P(SAMPLE_AXES, None, "space", None), P(), P())
    return jax.shard_map(shards, mesh=split, in_specs=in_specs, out_specs=out_specs, check_vma=False)
```

```python
import jax
import jax.numpy as jnp
from jax import lax
from jax.sharding import Mesh, PartitionSpec as P

ROWS = 4
COLS = 64


def extended(block, sides, width):
    for axis, dim in sides:
        count = lax.axis_size(axis)
        forward = [(i, i + 1) for i in range(count - 1)]
        backward = [(target, source) for source, target in forward]
        low = lax.ppermute(
            lax.slice_in_dim(block, block.shape[dim] - width, None, axis=dim), axis, forward
        )
        high = lax.ppermute(lax.slice_in_dim(block, 0, width, axis=dim), axis, backward)
        block = jnp.concatenate([low, block, high], axis=dim)
    return block


def shifted(planes, row_step, col_step, row_count, col_count):
    margin = col_count + 1
    widened = jnp.pad(planes, ((0, 0), (0, 0), (margin, margin)))
    offset = margin + row_step * col_count + col_step
    moved_cells = widened[:, :, offset : offset + row_count * col_count]
    column = jnp.arange(row_count * col_count) % col_count + col_step
    inside = (column >= 0) & (column < col_count)
    return jnp.where(inside, moved_cells, jnp.zeros_like(moved_cells))


def tap_patches(padded, depth_tap, row_tap, row_count, col_count):
    depth_len = padded.shape[1] - 2
    planes = padded[:, depth_tap : depth_tap + depth_len]
    stacked = jnp.stack(
        [shifted(planes, row_tap - 1, col_tap - 1, row_count, col_count) for col_tap in range(3)]
    )
    return stacked.reshape(3 * planes.shape[0], depth_len * planes.shape[2])


def conv_cube(padded, kernel, row_count, col_count):
    depth_len = padded.shape[1] - 2
    chans_in = kernel.shape[3]
    chans_out = kernel.shape[4]
    summed = jnp.zeros((chans_out, depth_len * padded.shape[2]), jnp.float32)
    for depth_tap in range(3):
        for row_tap in range(3):
            patches = tap_patches(padded, depth_tap, row_tap, row_count, col_count)
            tap_block = kernel[depth_tap, row_tap].reshape(3 * chans_in, chans_out)
            summed = summed + lax.dot_general(
                tap_block, patches, (((0,), (0,)), ((), ())), preferred_element_type=jnp.float32
            )
    return summed.reshape(chans_out, depth_len, padded.shape[2])


def weight_terms(padded, grad_out, row_count, col_count):
    chans_in = padded.shape[0]
    chans_out = grad_out.shape[0]
    flat_grad = grad_out.reshape(chans_out, -1)
    pieces = []
    for depth_tap in range(3):
        for row_tap in range(3):
            patches = tap_patches(padded, depth_tap, row_tap, row_count, col_count)
            pieces.append(
                lax.dot_general(
                    patches, flat_grad, (((1,), (1,)), ((), ())), preferred_element_type=jnp.float32
                )
            )
    return jnp.stack(pieces).reshape(3, 3, 3, chans_in, chans_out)


def flip_taps(kernel):
    return jnp.transpose(kernel[::-1, ::-1, ::-1], (0, 1, 2, 4, 3))


def pool_matrix(row_count, col_count):
    cells = jnp.arange(row_count * col_count)
    target = cells // col_count // 2 * (col_count // 2) + cells % col_count // 2
    return (target[:, None] == jnp.arange(row_count * col_count // 4)[None, :]).astype(jnp.float32)


def pool_cube(values, matrix):
    chans, depth_len, plane_len = values.shape
    paired = values.reshape(chans, depth_len // 2, 2, plane_len).sum(axis=2)
    return jnp.einsum("cdp,pq->cdq", paired, matrix, precision=lax.Precision.HIGHEST) * 0.125


def upsample_cube(values, matrix):
    spread = jnp.einsum("cdq,pq->cdp", values, matrix, precision=lax.Precision.HIGHEST)
    return jnp.repeat(spread, 2, axis=1)


def gelu_fwd(values):
    return jax.nn.gelu(values, approximate=True)


def gelu_back(pre_values, upstream):
    return jax.vjp(gelu_fwd, pre_values)[1](upstream)[0]


def extend(field, width):
    return extended(field, (("space", 1),), width)


def swap_add(parts, axis):
    me = lax.axis_index(axis)
    halves = parts.reshape(2, -1)
    own = lax.dynamic_index_in_dim(halves, me, 0, keepdims=False)
    other = lax.dynamic_index_in_dim(halves, 1 - me, 0, keepdims=False)
    return own + lax.ppermute(other, axis, [(0, 1), (1, 0)])


def swap_join(part, axis):
    me = lax.axis_index(axis)
    theirs = lax.ppermute(part, axis, [(0, 1), (1, 0)])
    first = jnp.where(me == 0, part, theirs)
    second = jnp.where(me == 0, theirs, part)
    return jnp.concatenate([first, second])


def mean_terms(terms, samples, rider):
    axes = ("rows", "z_high", "space")
    devices = lax.axis_size("rows") * lax.axis_size("z_high") * lax.axis_size("space")
    flat = jnp.concatenate([term.reshape(-1) for term in terms])
    total = flat.shape[0]
    padded = -(-total // (4 * devices)) * 4 * devices
    own = swap_add(jnp.pad(flat, (0, padded - total)), "core")
    own = swap_add(own, "x_low")
    own, rider = lax.optimization_barrier((own, rider))
    pieces = lax.all_to_all(own.reshape(devices, -1), axes, 0, 0, tiled=True)
    piece = (pieces.sum(axis=0) / samples).astype(jnp.bfloat16)
    spread = jnp.broadcast_to(piece, (devices,) + piece.shape)
    mine = lax.all_to_all(spread, axes, 0, 0, tiled=True).reshape(-1)
    pair = ("x_low", "core")
    quarters = [mine] + [
        lax.ppermute(mine, pair, [(i, i ^ flip) for i in range(4)]) for flip in (1, 2, 3)
    ]
    order = (jnp.arange(4) ^ (lax.axis_index("core") * 2 + lax.axis_index("x_low")))
    order = jnp.where(order == 1, 2, jnp.where(order == 2, 1, order))
    gathered = jnp.take(jnp.stack(quarters), order, axis=0).reshape(-1)
    gathered = gathered[:total].astype(jnp.float32)
    results = []
    start = 0
    for term in terms:
        results.append(gathered[start : start + term.size].reshape(term.shape))
        start += term.size
    return tuple(results), rider


def shards(activations, cotangent, weight_mid, weight_deep):
    row_count = ROWS
    col_count = COLS
    source = activations[0]
    matrix = pool_matrix(row_count, col_count)
    source_ext = extend(source, 1)
    mid_pre = conv_cube(source_ext, weight_mid, row_count, col_count)
    pooled_ext = extend(pool_cube(gelu_fwd(mid_pre), matrix).astype(jnp.bfloat16), 1)
    deep_pre = conv_cube(pooled_ext, weight_deep, row_count // 2, col_count // 2)
    deep_grad = gelu_back(deep_pre, cotangent[0].astype(jnp.float32)).astype(jnp.bfloat16)
    deep_terms = weight_terms(pooled_ext, deep_grad, row_count // 2, col_count // 2)
    samples = 1
    for axis in SAMPLE_AXES:
        samples *= lax.axis_size(axis)
    back_pooled = conv_cube(
        extend(deep_grad, 1), flip_taps(weight_deep), row_count // 2, col_count // 2
    )
    spread = upsample_cube(back_pooled, matrix) * 0.125
    mid_grad = gelu_back(mid_pre, spread).astype(jnp.bfloat16)
    mid_terms = weight_terms(source_ext, mid_grad, row_count, col_count)
    (grad_mid, grad_deep), mid_grad = mean_terms((mid_terms, deep_terms), samples, mid_grad)
    grad_input = conv_cube(extend(mid_grad, 1), flip_taps(weight_mid), row_count, col_count).astype(
        jnp.bfloat16
    )
    return (grad_input[None], grad_mid, grad_deep)


SAMPLE_AXES = ("rows", "x_low", "z_high", "core")


def solution(mesh):
    samples, slabs = mesh.devices.shape
    split = Mesh(mesh.devices.reshape(samples // 8, 2, 2, 2, slabs), SAMPLE_AXES + ("space",))
    in_specs = (P(SAMPLE_AXES, None, "space", None), P(SAMPLE_AXES, None, "space", None), P(), P())
    out_specs = (P(SAMPLE_AXES, None, "space", None), P(), P())
    return jax.shard_map(shards, mesh=split, in_specs=in_specs, out_specs=out_specs, check_vma=False)
```

```python
import jax
import jax.numpy as jnp
from jax import lax
from jax.sharding import Mesh, PartitionSpec as P

ROWS = 4
COLS = 64


def extended(block, sides, width):
    for axis, dim in sides:
        count = lax.axis_size(axis)
        forward = [(i, i + 1) for i in range(count - 1)]
        backward = [(target, source) for source, target in forward]
        low = lax.ppermute(
            lax.slice_in_dim(block, block.shape[dim] - width, None, axis=dim), axis, forward
        )
        high = lax.ppermute(lax.slice_in_dim(block, 0, width, axis=dim), axis, backward)
        block = jnp.concatenate([low, block, high], axis=dim)
    return block


def shifted(planes, row_step, col_step, row_count, col_count):
    margin = col_count + 1
    widened = jnp.pad(planes, ((0, 0), (0, 0), (margin, margin)))
    offset = margin + row_step * col_count + col_step
    moved_cells = widened[:, :, offset : offset + row_count * col_count]
    column = jnp.arange(row_count * col_count) % col_count + col_step
    inside = (column >= 0) & (column < col_count)
    return jnp.where(inside, moved_cells, jnp.zeros_like(moved_cells))


def tap_patches(padded, depth_tap, row_tap, row_count, col_count):
    depth_len = padded.shape[1] - 2
    planes = padded[:, depth_tap : depth_tap + depth_len]
    stacked = jnp.stack(
        [shifted(planes, row_tap - 1, col_tap - 1, row_count, col_count) for col_tap in range(3)]
    )
    return stacked.reshape(3 * planes.shape[0], depth_len * planes.shape[2])


def conv_cube(padded, kernel, row_count, col_count):
    depth_len = padded.shape[1] - 2
    chans_in = kernel.shape[3]
    chans_out = kernel.shape[4]
    summed = jnp.zeros((chans_out, depth_len * padded.shape[2]), jnp.float32)
    for depth_tap in range(3):
        for row_tap in range(3):
            patches = tap_patches(padded, depth_tap, row_tap, row_count, col_count)
            tap_block = kernel[depth_tap, row_tap].reshape(3 * chans_in, chans_out)
            summed = summed + lax.dot_general(
                tap_block, patches, (((0,), (0,)), ((), ())), preferred_element_type=jnp.float32
            )
    return summed.reshape(chans_out, depth_len, padded.shape[2])


def weight_terms(padded, grad_out, row_count, col_count):
    chans_in = padded.shape[0]
    chans_out = grad_out.shape[0]
    flat_grad = grad_out.reshape(chans_out, -1)
    pieces = []
    for depth_tap in range(3):
        for row_tap in range(3):
            patches = tap_patches(padded, depth_tap, row_tap, row_count, col_count)
            pieces.append(
                lax.dot_general(
                    patches, flat_grad, (((1,), (1,)), ((), ())), preferred_element_type=jnp.float32
                )
            )
    return jnp.stack(pieces).reshape(3, 3, 3, chans_in, chans_out)


def flip_taps(kernel):
    return jnp.transpose(kernel[::-1, ::-1, ::-1], (0, 1, 2, 4, 3))


def pool_matrix(row_count, col_count):
    cells = jnp.arange(row_count * col_count)
    target = cells // col_count // 2 * (col_count // 2) + cells % col_count // 2
    return (target[:, None] == jnp.arange(row_count * col_count // 4)[None, :]).astype(jnp.float32)


def pool_cube(values, matrix):
    chans, depth_len, plane_len = values.shape
    paired = values.reshape(chans, depth_len // 2, 2, plane_len).sum(axis=2)
    return jnp.einsum("cdp,pq->cdq", paired, matrix, precision=lax.Precision.HIGHEST) * 0.125


def upsample_cube(values, matrix):
    spread = jnp.einsum("cdq,pq->cdp", values, matrix, precision=lax.Precision.HIGHEST)
    return jnp.repeat(spread, 2, axis=1)


def gelu_fwd(values):
    return jax.nn.gelu(values, approximate=True)


def gelu_back(pre_values, upstream):
    return jax.vjp(gelu_fwd, pre_values)[1](upstream)[0]


def extend(field, width):
    return extended(field, (("space", 1),), width)


def swap_add(parts, axis):
    me = lax.axis_index(axis)
    halves = parts.reshape(2, -1)
    own = lax.dynamic_index_in_dim(halves, me, 0, keepdims=False)
    other = lax.dynamic_index_in_dim(halves, 1 - me, 0, keepdims=False)
    return own + lax.ppermute(other, axis, [(0, 1), (1, 0)])


def swap_join(part, axis):
    me = lax.axis_index(axis)
    theirs = lax.ppermute(part, axis, [(0, 1), (1, 0)])
    first = jnp.where(me == 0, part, theirs)
    second = jnp.where(me == 0, theirs, part)
    return jnp.concatenate([first, second])


def mean_terms(terms, samples, rider):
    axes = ("y_high", "x_high", "z_high", "space")
    devices = 1
    for axis in axes:
        devices *= lax.axis_size(axis)
    flat = jnp.concatenate([term.reshape(-1) for term in terms])
    total = flat.shape[0]
    padded = -(-total // (8 * devices)) * 8 * devices
    own = swap_add(jnp.pad(flat, (0, padded - total)), "core")
    own = swap_add(own, "x_low")
    own = swap_add(own, "y_low")
    own, rider = lax.optimization_barrier((own, rider))
    pieces = lax.all_to_all(own.reshape(devices, -1), axes, 0, 0, tiled=True)
    piece = (pieces.sum(axis=0) / samples).astype(jnp.bfloat16)
    spread = jnp.broadcast_to(piece, (devices,) + piece.shape)
    mine = lax.all_to_all(spread, axes, 0, 0, tiled=True).reshape(-1)
    gathered = swap_join(swap_join(swap_join(mine, "y_low"), "x_low"), "core")[:total].astype(jnp.float32)
    results = []
    start = 0
    for term in terms:
        results.append(gathered[start : start + term.size].reshape(term.shape))
        start += term.size
    return tuple(results), rider


def shards(activations, cotangent, weight_mid, weight_deep):
    row_count = ROWS
    col_count = COLS
    source = activations[0]
    matrix = pool_matrix(row_count, col_count)
    source_ext = extend(source, 1)
    mid_pre = conv_cube(source_ext, weight_mid, row_count, col_count)
    pooled_ext = extend(pool_cube(gelu_fwd(mid_pre), matrix).astype(jnp.bfloat16), 1)
    deep_pre = conv_cube(pooled_ext, weight_deep, row_count // 2, col_count // 2)
    deep_grad = gelu_back(deep_pre, cotangent[0].astype(jnp.float32)).astype(jnp.bfloat16)
    deep_terms = weight_terms(pooled_ext, deep_grad, row_count // 2, col_count // 2)
    samples = 1
    for axis in SAMPLE_AXES:
        samples *= lax.axis_size(axis)
    back_pooled = conv_cube(
        extend(deep_grad, 1), flip_taps(weight_deep), row_count // 2, col_count // 2
    )
    spread = upsample_cube(back_pooled, matrix) * 0.125
    mid_grad = gelu_back(mid_pre, spread).astype(jnp.bfloat16)
    mid_terms = weight_terms(source_ext, mid_grad, row_count, col_count)
    (grad_mid, grad_deep), mid_grad = mean_terms((mid_terms, deep_terms), samples, mid_grad)
    grad_input = conv_cube(extend(mid_grad, 1), flip_taps(weight_mid), row_count, col_count).astype(
        jnp.bfloat16
    )
    return (grad_input[None], grad_mid, grad_deep)


SAMPLE_AXES = ("y_high", "y_low", "x_high", "x_low", "z_high", "core")


def solution(mesh):
    samples, slabs = mesh.devices.shape
    split = Mesh(mesh.devices.reshape(samples // 32, 2, 2, 2, 2, 2, slabs), SAMPLE_AXES + ("space",))
    in_specs = (P(SAMPLE_AXES, None, "space", None), P(SAMPLE_AXES, None, "space", None), P(), P())
    out_specs = (P(SAMPLE_AXES, None, "space", None), P(), P())
    return jax.shard_map(shards, mesh=split, in_specs=in_specs, out_specs=out_specs, check_vma=False)
```
